256 devices in a mesh: ctx: 32 (over z, y), ch: 8 (over x, core).
Axes of the slice: x: 4, y: 4, z: 8, core: 2. Of those that a mesh axis runs over, the one named last changes fastest.
Arguments:
- streams: bfloat16 [3, 8192, 4096], P(None, 'ctx', 'ch'), may hold values from -6 to 6
- short_filters: float32 [3, 3, 4096], P(None, None, 'ch'), may hold values from -3.5 to 3.5
- long_filter: float32 [8192, 4096], P('ctx', 'ch'), may hold values from -0.069605824 to 0.069605824
- out_weight: bfloat16 [4096, 4096], P('ch'), may hold values from -0.09375 to 0.09375
Outputs:
- mixed: bfloat16 [8192, 4096], P('ctx', 'ch')
The draws below stay inside these ranges and needn't reach their ends.
All inputs are finite; a program needn't handle non-finite values.
Results may differ from the reference program's by a relative error of at most 0.005.
Values may be sent and summed in bfloat16 or wider, within the bound.
No kernel may reach another device: no remote copies, remote signals or barrier semaphores. Data moves between devices by JAX's collectives and lax.ppermute only.
A program may use at most 64 MiB of HBM per device.

```python
import math
import jax
import jax.numpy as jnp
from jax import lax

D = 4096
KERNEL = 3
SEQ = 8192


def draw_long_filter(key, part):
    key_noise, key_rates = jax.random.split(key, 2)
    tap_index = jnp.arange(SEQ, dtype=jnp.float32)[:, None]
    decay_rates = jnp.exp(jax.random.uniform(key_rates, (1, D), jnp.float32, math.log(0.3), math.log(3.0)))
    envelope = jnp.exp(-decay_rates * tap_index / SEQ) * (2.0 / SEQ) ** 0.5
    noise_draw = jax.random.truncated_normal(key_noise, -4.0, 4.0, (SEQ, D), jnp.float32)
    return noise_draw * envelope


def level_of(rng, extent, pieces, low, largest):
    def one(dim, parts):
        steps = jax.random.uniform(jax.random.fold_in(jax.random.fold_in(rng, 6), dim), (parts,), jnp.float32, low / len(pieces), largest / len(pieces))
        return jnp.repeat(jnp.exp(steps), extent[dim] // parts).reshape((-1,) + (1,) * (len(extent) - dim - 1))

    loudness = one(*pieces[0])
    for cut in pieces[1:]:
        loudness = loudness * one(*cut)
    return loudness


def gaussian(stream_key, dims, scale, limit, cuts=(), kind=jnp.bfloat16):
    values = scale * jax.random.normal(stream_key, dims, jnp.float32)
    if cuts:
        values = values * level_of(stream_key, dims, cuts, -0.22, 0.18)
    return jnp.clip(values, -limit, limit).astype(kind)


def setup_inputs(seed: int = 0) -> dict:
    streams_of = jax.random.split(jax.random.key(seed), 5)
    streams = gaussian(streams_of[0], (3, SEQ, D), 1.0, 6.0, ((1, 32), (2, 8)))
    short_filters = gaussian(streams_of[1], (3, KERNEL, D), KERNEL ** -0.5, 3.5, ((2, 8),), jnp.float32)
    long_filter = draw_long_filter(jax.random.fold_in(streams_of[4], 71), 0)
    out_weight = gaussian(streams_of[3], (D, D), D ** -0.5, 0.09375, ((0, 8),))
    return {"streams": streams, "short_filters": short_filters, "long_filter": long_filter, "out_weight": out_weight}


def featurize(streams, short_filters):
    kernel_size = short_filters.shape[1]
    seq_rows = streams.shape[1]
    padded = jnp.pad(streams.astype(jnp.float32), ((0, 0), (kernel_size - 1, 0), (0, 0)))
    summed = jnp.zeros(streams.shape, jnp.float32)
    for offset in range(kernel_size):
        start_row = kernel_size - 1 - offset
        summed = summed + short_filters[:, offset, None, :] * padded[:, start_row:start_row + seq_rows, :]
    return summed


def long_block(pair_items):
    signal_cols, filter_cols = pair_items
    length_full = 2 * signal_cols.shape[0]
    spectrum = jnp.fft.rfft(signal_cols, n=length_full, axis=0) * jnp.fft.rfft(filter_cols, n=length_full, axis=0)
    return jnp.fft.irfft(spectrum, n=length_full, axis=0)[: signal_cols.shape[0]]


def reference(streams, short_filters, long_filter, out_weight):
    features = featurize(streams, short_filters)
    signal_all = features[1] * features[2]
    block_cols = min(D, 512)
    groups = D // block_cols
    signal_blocks = signal_all.reshape(SEQ, groups, block_cols).transpose(1, 0, 2)
    filter_blocks = long_filter.reshape(SEQ, groups, block_cols).transpose(1, 0, 2)
    convolved = lax.map(long_block, (signal_blocks, filter_blocks))
    convolved = convolved.transpose(1, 0, 2).reshape(SEQ, D)
    gated_act = (features[0] * convolved).astype(jnp.bfloat16)
    return jnp.dot(gated_act, out_weight, preferred_element_type=jnp.float32).astype(jnp.bfloat16)
```

```python
import jax
import jax.numpy as jnp
from jax import lax
from jax.sharding import PartitionSpec as P


def to_channel_owners(block):
    devices = lax.axis_size("ctx")
    lead = block.shape[:-2]
    rows, channels = block.shape[-2:]
    share = channels // devices
    by_channel = jnp.swapaxes(block, -1, -2).reshape(lead + (devices, share, rows))
    arrived = lax.all_to_all(by_channel, "ctx", split_axis=len(lead), concat_axis=len(lead), tiled=True)
    arrived = jnp.swapaxes(arrived, len(lead), len(lead) + 1)
    return arrived.reshape(lead + (share, devices * rows))


def to_position_owners(block, rows):
    devices = lax.axis_size("ctx")
    share = block.shape[0]
    by_rows = jnp.swapaxes(block.reshape(share, devices, rows), 0, 1)
    arrived = lax.all_to_all(by_rows, "ctx", split_axis=0, concat_axis=0, tiled=True)
    return arrived.reshape(devices * share, rows)


def featurize(streams, taps):
    kernel_size = taps.shape[1]
    seq = streams.shape[-1]
    padded = jnp.pad(streams, ((0, 0), (0, 0), (kernel_size - 1, 0)))
    summed = jnp.zeros(streams.shape, jnp.float32)
    for offset in range(kernel_size):
        start = kernel_size - 1 - offset
        summed = summed + taps[:, offset, :, None] * padded[:, :, start : start + seq]
    return summed


def long_conv(signal, taps):
    seq = signal.shape[-1]
    full = 2 * seq
    spectrum = jnp.fft.rfft(signal, n=full, axis=-1) * jnp.fft.rfft(taps, n=full, axis=-1)
    return jnp.fft.irfft(spectrum, n=full, axis=-1)[..., :seq]


def on_device(streams, short_filters, long_filter, out_weight):
    devices = lax.axis_size("ctx")
    rows = streams.shape[1]
    channels = streams.shape[2]
    share = channels // devices
    me = lax.axis_index("ctx")
    local_streams = to_channel_owners(streams)
    local_filter = to_channel_owners(long_filter)
    taps = lax.dynamic_slice_in_dim(short_filters, me * share, share, axis=2)
    features = featurize(local_streams.astype(jnp.float32), taps)
    signal = features[1] * features[2]
    convolved = long_conv(signal, local_filter)
    gated_local = (features[0] * convolved).astype(jnp.bfloat16)
    gated = to_position_owners(gated_local, rows)
    partial = lax.dot_general(
        gated, out_weight, (((0,), (0,)), ((), ())), preferred_element_type=jnp.float32
    )
    summed = lax.psum_scatter(partial, "ch", scatter_dimension=1, tiled=True)
    return summed.astype(jnp.bfloat16)


def solution(mesh):
    return jax.shard_map(
        on_device,
        mesh=mesh,
        in_specs=(P(None, "ctx", "ch"), P(None, None, "ch"), P("ctx", "ch"), P("ch", None)),
        out_specs=P("ctx", "ch"),
        check_vma=False,
    )
```

```python
import math

import jax
import jax.numpy as jnp
from jax import lax
from jax.sharding import PartitionSpec as P

HIGHEST = lax.Precision.HIGHEST


def to_channel_owners(block):
    devices = lax.axis_size("ctx")
    lead = block.shape[:-2]
    rows, channels = block.shape[-2:]
    share = channels // devices
    by_channel = jnp.swapaxes(block, -1, -2).reshape(lead + (devices, share, rows))
    arrived = lax.all_to_all(by_channel, "ctx", split_axis=len(lead), concat_axis=len(lead), tiled=True)
    arrived = jnp.swapaxes(arrived, len(lead), len(lead) + 1)
    return arrived.reshape(lead + (share, devices * rows))


def to_position_owners(block, rows):
    devices = lax.axis_size("ctx")
    share = block.shape[0]
    by_rows = jnp.swapaxes(block.reshape(share, devices, rows), 0, 1)
    arrived = lax.all_to_all(by_rows, "ctx", split_axis=0, concat_axis=0, tiled=True)
    return arrived.reshape(devices * share, rows)


def featurize(streams, taps):
    kernel_size = taps.shape[1]
    seq = streams.shape[-1]
    padded = jnp.pad(streams, ((0, 0), (0, 0), (kernel_size - 1, 0)))
    summed = jnp.zeros(streams.shape, jnp.float32)
    for offset in range(kernel_size):
        start = kernel_size - 1 - offset
        summed = summed + taps[:, offset, :, None] * padded[:, :, start : start + seq]
    return summed


def angle_table(left_ids, right_ids, period):
    product_ids = left_ids * right_ids % period
    return (2.0 * math.pi / period) * product_ids.astype(jnp.float32)


def long_conv(signal, taps):
    channels, seq = signal.shape
    full = 2 * seq
    radix = math.isqrt(full)
    half = seq // radix
    ids = jnp.arange(radix, dtype=jnp.int32)
    small = angle_table(ids[:, None], ids[None, :], radix)
    cos_small, sin_small = jnp.cos(small), jnp.sin(small)
    turn = angle_table(ids[:, None], ids[None, :], full)
    cos_turn, sin_turn = jnp.cos(turn)[:, None, :], jnp.sin(turn)[:, None, :]
    both = jnp.stack([signal, taps]).reshape(2, channels, half, radix)
    first = jnp.concatenate([cos_small[:, :half], -sin_small[:, :half]], axis=0)
    stage = jnp.einsum("ka,scab->skcb", first, both, precision=HIGHEST)
    part_real, part_imag = stage[:, :radix], stage[:, radix:]
    turned = jnp.concatenate(
        [part_real * cos_turn + part_imag * sin_turn, part_imag * cos_turn - part_real * sin_turn], axis=-1
    )
    forward = jnp.block([[cos_small, -sin_small], [sin_small, cos_small]])
    spectra = jnp.einsum("skcb,bd->skcd", turned, forward, precision=HIGHEST)
    sr, si = spectra[..., :radix], spectra[..., radix:]
    prod = jnp.concatenate([sr[0] * sr[1] - si[0] * si[1], sr[0] * si[1] + si[0] * sr[1]], axis=-1)
    backward = jnp.block([[cos_small, sin_small], [-sin_small, cos_small]])
    back = jnp.einsum("kcd,db->kcb", prod, backward, precision=HIGHEST)
    br, bi = back[..., :radix], back[..., radix:]
    unturned_real = br * cos_turn - bi * sin_turn
    unturned_imag = bi * cos_turn + br * sin_turn
    out = jnp.einsum("ak,kcb->cab", cos_small[:half], unturned_real, precision=HIGHEST) - jnp.einsum(
        "ak,kcb->cab", sin_small[:half], unturned_imag, precision=HIGHEST
    )
    return out.reshape(channels, seq) * (1.0 / full)


def on_device(streams, short_filters, long_filter, out_weight):
    devices = lax.axis_size("ctx")
    rows = streams.shape[1]
    channels = streams.shape[2]
    share = channels // devices
    me = lax.axis_index("ctx")
    local_streams = to_channel_owners(streams)
    local_filter = to_channel_owners(long_filter)
    taps = lax.dynamic_slice_in_dim(short_filters, me * share, share, axis=2)
    features = featurize(local_streams.astype(jnp.float32), taps)
    signal = features[1] * features[2]
    convolved = long_conv(signal, local_filter)
    gated_local = (features[0] * convolved).astype(jnp.bfloat16)
    gated = to_position_owners(gated_local, rows)
    partial = lax.dot_general(
        gated, out_weight, (((0,), (0,)), ((), ())), preferred_element_type=jnp.float32
    )
    summed = lax.psum_scatter(partial, "ch", scatter_dimension=1, tiled=True)
    return summed.astype(jnp.bfloat16)


def solution(mesh):
    return jax.shard_map(
        on_device,
        mesh=mesh,
        in_specs=(P(None, "ctx", "ch"), P(None, None, "ch"), P("ctx", "ch"), P("ch", None)),
        out_specs=P("ctx", "ch"),
        check_vma=False,
    )
```
